256 devices in a mesh: wide: 32 (over x_lo, z, core), tm: 8 (over x_hi, y).
Axes of the slice: x: 4 (x_hi: 2, x_lo: 2; x = x_hi * 2 + x_lo), y: 4, z: 8, core: 2. Of those that a mesh axis runs over, the one named last changes fastest.
Arguments:
- voltages: int32 [256, 524288], P('wide', 'tm'), may hold values from -128 to 127
- taps: int32 [16, 1024], replicated, may hold values from -32 to 32
Outputs:
- visibility: float32 [256, 2, 512, 256], P('tm', None, 'wide')
The draws below stay inside these ranges and needn't reach their ends.
All inputs are finite; a program needn't handle non-finite values.
Results may differ from the reference program's by a relative error of at most 0.0024.
Values may be sent and summed in bfloat16 or wider, within the bound.
No kernel may reach another device: no remote copies, remote signals or barrier semaphores. Data moves between devices by JAX's collectives and lax.ppermute only.
A program may use at most 64 MiB of HBM per device.

```python
import jax
import jax.numpy as jnp
from jax import lax

A = 256
C = 512
P_SIZE = 16
L = 1024
NSPEC = 512
SAMPLES = 524288


def place_ends(array, key, least, top_value):
    index_at = [jax.random.randint(jax.random.fold_in(key, axis), (), 0, length) for axis, length in enumerate(array.shape)]
    widest = array.shape.index(max(array.shape))
    next_to = index_at[:widest] + [(index_at[widest] + 1) % array.shape[widest]] + index_at[widest + 1:]
    return array.at[tuple(index_at)].set(least).at[tuple(next_to)].set(top_value)


def setup_inputs(seed: int = 0) -> dict:
    key_of = jax.random.split(jax.random.key(seed), 3)
    voltages = place_ends(jax.random.randint(key_of[0], (A, SAMPLES), -128, 128), jax.random.fold_in(key_of[0], 1), -128, 127).astype(jnp.int32)
    taps = place_ends(jax.random.randint(key_of[1], (P_SIZE, L), -32, 33), jax.random.fold_in(key_of[1], 1), -32, 32).astype(jnp.int32)
    return {"voltages": voltages, "taps": taps}


FIR_SCALE = 2.0 ** -12


def channelize(volt_row, taps_float):
    frames = volt_row.astype(jnp.bfloat16).astype(jnp.float32).reshape(NSPEC, L)
    padded = jnp.concatenate([jnp.zeros((P_SIZE - 1, L), jnp.float32), frames], axis=0)
    filtered = jnp.zeros((NSPEC, L), jnp.float32)
    for lag in range(P_SIZE):
        filtered = filtered + taps_float[lag] * padded[P_SIZE - 1 - lag:P_SIZE - 1 - lag + NSPEC]
    filtered = filtered * FIR_SCALE
    spectrum = jnp.fft.rfft(filtered, axis=-1)[:, :C] * (L ** -0.5)
    real_part = jnp.real(spectrum).astype(jnp.bfloat16)
    imag_part = jnp.imag(spectrum).astype(jnp.bfloat16)
    return jnp.concatenate([real_part.T, imag_part.T], axis=1)


def channel_gram(full_rows):
    full_float = full_rows.astype(jnp.float32)
    rotated = jnp.concatenate([full_float[:, NSPEC:], -full_float[:, :NSPEC]], axis=1)
    real_part = jnp.dot(full_float, full_float.T, preferred_element_type=jnp.float32)
    imag_part = jnp.dot(rotated, full_float.T, preferred_element_type=jnp.float32)
    return jnp.stack([real_part, imag_part], axis=0)


def reference(voltages, taps):
    taps_float = taps.astype(jnp.float32)
    spectra = lax.map(lambda volt_row: channelize(volt_row, taps_float), voltages)
    per_channel = lax.map(channel_gram, jnp.transpose(spectra, (1, 0, 2)))
    return jnp.transpose(per_channel, (2, 1, 0, 3)) * (1.0 / NSPEC)
```

```python
import numpy as np
import jax
import jax.numpy as jnp
from jax import lax
from jax.sharding import PartitionSpec as P

FIR_SCALE = 2.0 ** (-12)


def shifted(array, axis, by):
    devices = lax.axis_size(axis)
    pairs = [(i, i + by) for i in range(devices) if 0 <= i + by < devices]
    return lax.ppermute(array, axis, pairs)


def dft_factors(length, channels, split):
    hi = np.arange(length // split)[:, None] * split * np.arange(channels)[None, :] % length
    lo = np.arange(split)[:, None] * np.arange(channels)[None, :] % length
    ang_hi = 2.0 * np.pi / length * hi
    ang_lo = 2.0 * np.pi / length * lo
    return (
        np.cos(ang_hi).astype(np.float32),
        (-np.sin(ang_hi)).astype(np.float32),
        np.cos(ang_lo).astype(np.float32),
        (-np.sin(ang_lo)).astype(np.float32),
    )


def dft_table(length, channels):
    split = 32
    ch, sh, cl, sl = (jnp.asarray(t) for t in dft_factors(length, channels, split))
    re = ch[:, None, :] * cl[None, :, :] - sh[:, None, :] * sl[None, :, :]
    im = ch[:, None, :] * sl[None, :, :] + sh[:, None, :] * cl[None, :, :]
    table = jnp.stack([re, im], axis=2).reshape(length, 2, channels)
    return table * length ** (-0.5)


def shards(voltages, taps):
    local_inputs = voltages.shape[0]
    length = taps.shape[1]
    lags = taps.shape[0]
    spectra_dev = voltages.shape[1] // length
    channels = length // 2
    widen = lax.axis_size("wide")
    ranks = lax.axis_size("tm")
    groups = widen * ranks
    per_group = channels // groups

    frames = voltages.reshape(local_inputs, spectra_dev, length).transpose(1, 0, 2)
    frames = frames.astype(jnp.bfloat16)
    previous = shifted(frames[spectra_dev - (lags - 1) :], "tm", 1)
    extended = jnp.concatenate([previous, frames], axis=0).astype(jnp.float32)
    taps_float = taps.astype(jnp.float32)
    filtered = taps_float[0] * extended[lags - 1 : lags - 1 + spectra_dev]
    for lag in range(1, lags):
        filtered = filtered + taps_float[lag] * extended[lags - 1 - lag : lags - 1 - lag + spectra_dev]
    filtered = filtered * FIR_SCALE

    table = dft_table(length, channels)
    spectra = jnp.einsum(
        "sin,nrk->kirs",
        filtered,
        table,
        precision=lax.Precision.HIGHEST,
        preferred_element_type=jnp.float32,
    ).astype(jnp.bfloat16)
    packed = spectra.reshape(groups, per_group, local_inputs, 2, spectra_dev)
    got = lax.all_to_all(packed, ("wide", "tm"), 0, 0, tiled=True)
    got = got.reshape(widen, ranks, per_group, local_inputs, 2, spectra_dev)
    got = got.transpose(2, 0, 3, 1, 4, 5)
    rotated = jnp.stack([got[..., 1, :], -got[..., 0, :]], axis=-2)
    inputs = widen * local_inputs
    depth = ranks * 2 * spectra_dev
    full = got.reshape(per_group, inputs, depth)
    rotated = rotated.reshape(per_group, inputs, depth)
    real_part = jnp.einsum("cak,cbk->acb", full, full, preferred_element_type=jnp.float32)
    imag_part = jnp.einsum("cak,cbk->acb", rotated, full, preferred_element_type=jnp.float32)
    norm_factor = 1.0 / (spectra_dev * ranks)
    grams = jnp.stack([real_part, imag_part], axis=1) * norm_factor
    return lax.all_to_all(grams, "tm", 0, 2, tiled=True)


def solution(mesh):
    placed = (P("wide", "tm"), P())
    return jax.shard_map(
        shards, mesh=mesh, in_specs=placed, out_specs=P("tm", None, "wide", None), check_vma=False
    )
```

```python
import numpy as np
import jax
import jax.numpy as jnp
from jax import lax
from jax.experimental import pallas as pl
from jax.experimental.pallas import tpu as pltpu
from jax.sharding import PartitionSpec as P

FIR_SCALE = 2.0 ** (-12)


def shifted(array, axis, by):
    devices = lax.axis_size(axis)
    pairs = [(i, i + by) for i in range(devices) if 0 <= i + by < devices]
    return lax.ppermute(array, axis, pairs)


def dft_factors(length, channels, split):
    hi = np.arange(length // split)[:, None] * split * np.arange(channels)[None, :] % length
    lo = np.arange(split)[:, None] * np.arange(channels)[None, :] % length
    ang_hi = 2.0 * np.pi / length * hi
    ang_lo = 2.0 * np.pi / length * lo
    return (
        np.cos(ang_hi).astype(np.float32),
        (-np.sin(ang_hi)).astype(np.float32),
        np.cos(ang_lo).astype(np.float32),
        (-np.sin(ang_lo)).astype(np.float32),
    )


def dft_table(length, channels):
    split = 32
    ch, sh, cl, sl = (jnp.asarray(t) for t in dft_factors(length, channels, split))
    re = ch[:, None, :] * cl[None, :, :] - sh[:, None, :] * sl[None, :, :]
    im = ch[:, None, :] * sl[None, :, :] + sh[:, None, :] * cl[None, :, :]
    table = jnp.stack([re, im], axis=2).reshape(length, 2, channels)
    return table * length ** (-0.5)


def shards(voltages, taps):
    local_inputs = voltages.shape[0]
    length = taps.shape[1]
    lags = taps.shape[0]
    spectra_dev = voltages.shape[1] // length
    channels = length // 2
    widen = lax.axis_size("wide")
    ranks = lax.axis_size("tm")
    groups = widen * ranks
    per_group = channels // groups

    frames = voltages.reshape(local_inputs, spectra_dev, length).transpose(1, 0, 2)
    frames = frames.astype(jnp.bfloat16)
    previous = shifted(frames[spectra_dev - (lags - 1) :], "tm", 1)
    extended = jnp.concatenate([previous, frames], axis=0).astype(jnp.float32)
    taps_float = taps.astype(jnp.float32)
    filtered = taps_float[0] * extended[lags - 1 : lags - 1 + spectra_dev]
    for lag in range(1, lags):
        filtered = filtered + taps_float[lag] * extended[lags - 1 - lag : lags - 1 - lag + spectra_dev]
    filtered = filtered * FIR_SCALE

    table = dft_table(length, channels)
    spectra = jnp.einsum(
        "sin,nrk->kirs",
        filtered,
        table,
        precision=lax.Precision.HIGH,
        preferred_element_type=jnp.float32,
    ).astype(jnp.bfloat16)
    packed = spectra.reshape(groups, per_group, local_inputs, 2, spectra_dev)
    got = lax.all_to_all(packed, ("wide", "tm"), 0, 0, tiled=True)
    got = got.reshape(widen, ranks, per_group, local_inputs, 2 * spectra_dev).astype(jnp.float32)
    norm_factor = 1.0 / (spectra_dev * ranks)
    grams = channel_grams(got, norm_factor)
    back = lax.all_to_all(grams, "tm", 0, 0, tiled=True)
    rows = back.shape[3]
    return back.transpose(3, 1, 0, 2, 4).reshape(rows, 2, ranks * per_group, back.shape[4])


def gram_kernel(scale, x_ref, o_ref):
    widen, ranks, groups, local_inputs, depth = x_ref.shape
    inputs = widen * local_inputs
    half = depth // 2
    lane = lax.broadcasted_iota(jnp.int32, (inputs, depth), 1)
    sign = jnp.where(lane < half, -1.0, 1.0).astype(jnp.float32)
    rows = inputs // ranks
    for c in range(groups):
        acc = jnp.zeros((inputs, 2 * inputs), jnp.float32)
        for t in range(ranks):
            x = x_ref[:, t, c, :, :].reshape(inputs, depth)
            rot = pltpu.roll(x, half, 1) * sign
            y = jnp.concatenate([x, rot], axis=0).astype(jnp.bfloat16)
            acc = acc + lax.dot_general(
                x.astype(jnp.bfloat16), y, (((1,), (1,)), ((), ())),
                preferred_element_type=jnp.float32,
            )
        acc = acc * scale
        o_ref[:, 0, c, :, :] = acc[:, :inputs].reshape(ranks, rows, inputs)
        o_ref[:, 1, c, :, :] = acc[:, inputs:].reshape(ranks, rows, inputs)


def channel_grams(got, scale):
    widen, ranks, groups, local_inputs, depth = got.shape
    inputs = widen * local_inputs
    rows = inputs // ranks
    flops = 2 * groups * ranks * inputs * 2 * inputs * depth
    return pl.pallas_call(
        lambda x_ref, o_ref: gram_kernel(scale, x_ref, o_ref),
        out_shape=jax.ShapeDtypeStruct((ranks, 2, groups, rows, inputs), jnp.float32),
        in_specs=[pl.BlockSpec(memory_space=pltpu.VMEM)],
        out_specs=pl.BlockSpec(memory_space=pltpu.VMEM),
        cost_estimate=pl.CostEstimate(
            flops=flops, transcendentals=0, bytes_accessed=got.size * 4 + 2 * groups * inputs * inputs * 4
        ),
    )(got)


def solution(mesh):
    placed = (P("wide", "tm"), P())
    return jax.shard_map(
        shards, mesh=mesh, in_specs=placed, out_specs=P("tm", None, "wide", None), check_vma=False
    )
```

```python
import numpy as np
import jax
import jax.numpy as jnp
from jax import lax
from jax.experimental import pallas as pl
from jax.experimental.pallas import tpu as pltpu
from jax.sharding import PartitionSpec as P

FIR_SCALE = 2.0 ** (-12)


def shifted(array, axis, by):
    devices = lax.axis_size(axis)
    pairs = [(i, i + by) for i in range(devices) if 0 <= i + by < devices]
    return lax.ppermute(array, axis, pairs)


def dft_factors(length, channels, split):
    hi = np.arange(length // split)[:, None] * split * np.arange(channels)[None, :] % length
    lo = np.arange(split)[:, None] * np.arange(channels)[None, :] % length
    ang_hi = 2.0 * np.pi / length * hi
    ang_lo = 2.0 * np.pi / length * lo
    return (
        np.cos(ang_hi).astype(np.float32),
        (-np.sin(ang_hi)).astype(np.float32),
        np.cos(ang_lo).astype(np.float32),
        (-np.sin(ang_lo)).astype(np.float32),
    )


def dft_table(length, channels):
    split = 32
    ch, sh, cl, sl = (jnp.asarray(t) for t in dft_factors(length, channels, split))
    re = ch[:, None, :] * cl[None, :, :] - sh[:, None, :] * sl[None, :, :]
    im = ch[:, None, :] * sl[None, :, :] + sh[:, None, :] * cl[None, :, :]
    table = jnp.stack([re, im], axis=2).reshape(length, 2, channels)
    return table * length ** (-0.5)


def shards(voltages, taps):
    local_inputs = voltages.shape[0]
    length = taps.shape[1]
    lags = taps.shape[0]
    spectra_dev = voltages.shape[1] // length
    channels = length // 2
    widen = lax.axis_size("wide")
    ranks = lax.axis_size("tm")
    groups = widen * ranks
    per_group = channels // groups

    frames = voltages.reshape(local_inputs, spectra_dev, length).transpose(1, 0, 2)
    frames = frames.astype(jnp.bfloat16)
    previous = shifted(frames[spectra_dev - (lags - 1) :], "tm", 1)
    extended = jnp.concatenate([previous, frames], axis=0).astype(jnp.float32)
    taps_float = taps.astype(jnp.float32)
    filtered = taps_float[0] * extended[lags - 1 : lags - 1 + spectra_dev]
    for lag in range(1, lags):
        filtered = filtered + taps_float[lag] * extended[lags - 1 - lag : lags - 1 - lag + spectra_dev]
    filtered = filtered * FIR_SCALE

    table = dft_table(length, channels)
    spectra = jnp.einsum(
        "sin,nrk->kirs",
        filtered,
        table,
        precision=lax.Precision.HIGH,
        preferred_element_type=jnp.float32,
    ).astype(jnp.bfloat16)
    packed = spectra.reshape(groups, per_group * local_inputs, 2 * spectra_dev)
    got = lax.all_to_all(packed, ("wide", "tm"), 0, 0, tiled=True)
    got = got.reshape(widen, ranks, per_group * local_inputs, 2 * spectra_dev)
    norm_factor = 1.0 / (spectra_dev * ranks)
    grams = channel_grams(got, norm_factor, per_group)
    back = lax.all_to_all(grams, "tm", 0, 0, tiled=True)
    rows = back.shape[3]
    return back.transpose(3, 1, 0, 2, 4).reshape(rows, 2, ranks * per_group, back.shape[4])


def gram_kernel(scale, x_ref, o_ref):
    widen, ranks, stacked, depth = x_ref.shape
    groups = o_ref.shape[2]
    local_inputs = stacked // groups
    inputs = widen * local_inputs
    half = depth // 2
    lane = lax.broadcasted_iota(jnp.int32, (inputs, depth), 1)
    sign = jnp.where(lane < half, -1.0, 1.0).astype(jnp.float32)
    rows = inputs // ranks
    accs = [jnp.zeros((inputs, 2 * inputs), jnp.float32) for _ in range(groups)]
    for t in range(ranks):
        block = x_ref[:, t, :, :].astype(jnp.float32)
        for c in range(groups):
            x = block[:, c * local_inputs : (c + 1) * local_inputs, :].reshape(inputs, depth)
            rot = pltpu.roll(x, half, 1) * sign
            y = jnp.concatenate([x, rot], axis=0).astype(jnp.bfloat16)
            accs[c] = accs[c] + lax.dot_general(
                x.astype(jnp.bfloat16), y, (((1,), (1,)), ((), ())),
                preferred_element_type=jnp.float32,
            )
    for c in range(groups):
        acc = accs[c] * scale
        o_ref[:, 0, c, :, :] = acc[:, :inputs].reshape(ranks, rows, inputs)
        o_ref[:, 1, c, :, :] = acc[:, inputs:].reshape(ranks, rows, inputs)


def channel_grams(got, scale, groups):
    widen, ranks, stacked, depth = got.shape
    inputs = widen * stacked // groups
    rows = inputs // ranks
    flops = 2 * groups * ranks * inputs * 2 * inputs * depth
    return pl.pallas_call(
        lambda x_ref, o_ref: gram_kernel(scale, x_ref, o_ref),
        out_shape=jax.ShapeDtypeStruct((ranks, 2, groups, rows, inputs), jnp.float32),
        in_specs=[pl.BlockSpec(memory_space=pltpu.VMEM)],
        out_specs=pl.BlockSpec(memory_space=pltpu.VMEM),
        cost_estimate=pl.CostEstimate(
            flops=flops, transcendentals=0, bytes_accessed=got.size * 2 + 2 * groups * inputs * inputs * 4
        ),
    )(got)


def solution(mesh):
    placed = (P("wide", "tm"), P())
    return jax.shard_map(
        shards, mesh=mesh, in_specs=placed, out_specs=P("tm", None, "wide", None), check_vma=False
    )
```

```python
import numpy as np
import jax
import jax.numpy as jnp
from jax import lax
from jax.experimental import pallas as pl
from jax.experimental.pallas import tpu as pltpu
from jax.sharding import PartitionSpec as P

FIR_SCALE = 2.0 ** (-12)


def shifted(array, axis, by):
    devices = lax.axis_size(axis)
    pairs = [(i, i + by) for i in range(devices) if 0 <= i + by < devices]
    return lax.ppermute(array, axis, pairs)


def dft_factors(length, channels, split):
    hi = np.arange(length // split)[:, None] * split * np.arange(channels)[None, :] % length
    lo = np.arange(split)[:, None] * np.arange(channels)[None, :] % length
    ang_hi = 2.0 * np.pi / length * hi
    ang_lo = 2.0 * np.pi / length * lo
    return (
        np.cos(ang_hi).astype(np.float32),
        (-np.sin(ang_hi)).astype(np.float32),
        np.cos(ang_lo).astype(np.float32),
        (-np.sin(ang_lo)).astype(np.float32),
    )


def dft_table(length, channels):
    split = 32
    ch, sh, cl, sl = (jnp.asarray(t) for t in dft_factors(length, channels, split))
    re = ch[:, None, :] * cl[None, :, :] - sh[:, None, :] * sl[None, :, :]
    im = ch[:, None, :] * sl[None, :, :] + sh[:, None, :] * cl[None, :, :]
    table = jnp.stack([re, im], axis=2).reshape(length, 2, channels)
    return table * length ** (-0.5)


def shards(voltages, taps):
    local_inputs = voltages.shape[0]
    length = taps.shape[1]
    lags = taps.shape[0]
    spectra_dev = voltages.shape[1] // length
    channels = length // 2
    widen = lax.axis_size("wide")
    ranks = lax.axis_size("tm")
    groups = widen * ranks
    per_group = channels // groups

    frames = voltages.reshape(local_inputs, spectra_dev, length).transpose(1, 0, 2)
    frames = frames.astype(jnp.bfloat16)
    previous = shifted(frames[spectra_dev - (lags - 1) :], "tm", 1)
    taps_float = taps.astype(jnp.float32)
    table = dft_table(length, channels)

    def channelize(extended, count):
        extended = extended.astype(jnp.float32)
        filtered = taps_float[0] * extended[lags - 1 : lags - 1 + count]
        for lag in range(1, lags):
            filtered = filtered + taps_float[lag] * extended[lags - 1 - lag : lags - 1 - lag + count]
        filtered = filtered * FIR_SCALE
        return [
            jnp.einsum(
                "sin,nk->kis",
                filtered,
                table[:, part, :],
                precision=lax.Precision.HIGH,
                preferred_element_type=jnp.float32,
            ).astype(jnp.bfloat16)
            for part in range(2)
        ]

    later = channelize(frames, spectra_dev - (lags - 1))
    head = channelize(jnp.concatenate([previous, frames[: 2 * (lags - 1)]], axis=0), lags - 1)
    spectra = jnp.concatenate([head[0], later[0], head[1], later[1]], axis=-1)
    packed = spectra.reshape(groups, per_group * local_inputs, 2 * spectra_dev)
    got = lax.all_to_all(packed, ("wide", "tm"), 0, 0, tiled=True)
    got = got.reshape(widen, ranks, per_group * local_inputs, 2 * spectra_dev)
    norm_factor = 1.0 / (spectra_dev * ranks)
    grams = channel_grams(got, norm_factor, per_group)
    back = lax.all_to_all(grams, "tm", 0, 0, tiled=True)
    rows = back.shape[3]
    return back.transpose(3, 1, 0, 2, 4).reshape(rows, 2, ranks * per_group, back.shape[4])


def gram_kernel(scale, x_ref, o_ref):
    widen, ranks, stacked, depth = x_ref.shape
    groups = o_ref.shape[2]
    local_inputs = stacked // groups
    inputs = widen * local_inputs
    half = depth // 2
    lane = lax.broadcasted_iota(jnp.int32, (inputs, depth), 1)
    sign = jnp.where(lane < half, -1.0, 1.0).astype(jnp.float32)
    rows = inputs // ranks
    accs = [jnp.zeros((inputs, 2 * inputs), jnp.float32) for _ in range(groups)]
    for t in range(ranks):
        block = x_ref[:, t, :, :].astype(jnp.float32)
        for c in range(groups):
            x = block[:, c * local_inputs : (c + 1) * local_inputs, :].reshape(inputs, depth)
            rot = pltpu.roll(x, half, 1) * sign
            y = jnp.concatenate([x, rot], axis=0).astype(jnp.bfloat16)
            accs[c] = accs[c] + lax.dot_general(
                x.astype(jnp.bfloat16), y, (((1,), (1,)), ((), ())),
                preferred_element_type=jnp.float32,
            )
    for c in range(groups):
        acc = accs[c] * scale
        o_ref[:, 0, c, :, :] = acc[:, :inputs].reshape(ranks, rows, inputs)
        o_ref[:, 1, c, :, :] = acc[:, inputs:].reshape(ranks, rows, inputs)


def channel_grams(got, scale, groups):
    widen, ranks, stacked, depth = got.shape
    inputs = widen * stacked // groups
    rows = inputs // ranks
    flops = 2 * groups * ranks * inputs * 2 * inputs * depth
    return pl.pallas_call(
        lambda x_ref, o_ref: gram_kernel(scale, x_ref, o_ref),
        out_shape=jax.ShapeDtypeStruct((ranks, 2, groups, rows, inputs), jnp.float32),
        in_specs=[pl.BlockSpec(memory_space=pltpu.VMEM)],
        out_specs=pl.BlockSpec(memory_space=pltpu.VMEM),
        cost_estimate=pl.CostEstimate(
            flops=flops, transcendentals=0, bytes_accessed=got.size * 2 + 2 * groups * inputs * inputs * 4
        ),
    )(got)


def solution(mesh):
    placed = (P("wide", "tm"), P())
    return jax.shard_map(
        shards, mesh=mesh, in_specs=placed, out_specs=P("tm", None, "wide", None), check_vma=False
    )
```

```python
import numpy as np
import jax
import jax.numpy as jnp
from jax import lax
from jax.experimental import pallas as pl
from jax.experimental.pallas import tpu as pltpu
from jax.sharding import PartitionSpec as P

FIR_SCALE = 2.0 ** (-12)


def shifted(array, axis, by):
    devices = lax.axis_size(axis)
    pairs = [(i, i + by) for i in range(devices) if 0 <= i + by < devices]
    return lax.ppermute(array, axis, pairs)


def dft_factors(length, channels, split):
    hi = np.arange(length // split)[:, None] * split * np.arange(channels)[None, :] % length
    lo = np.arange(split)[:, None] * np.arange(channels)[None, :] % length
    ang_hi = 2.0 * np.pi / length * hi
    ang_lo = 2.0 * np.pi / length * lo
    return (
        np.cos(ang_hi).astype(np.float32),
        (-np.sin(ang_hi)).astype(np.float32),
        np.cos(ang_lo).astype(np.float32),
        (-np.sin(ang_lo)).astype(np.float32),
    )


def dft_table(length, channels):
    split = 32
    ch, sh, cl, sl = (jnp.asarray(t) for t in dft_factors(length, channels, split))
    re = ch[:, None, :] * cl[None, :, :] - sh[:, None, :] * sl[None, :, :]
    im = ch[:, None, :] * sl[None, :, :] + sh[:, None, :] * cl[None, :, :]
    table = jnp.stack([re, im], axis=2).reshape(length, 2, channels)
    return table * length ** (-0.5)


def shards(voltages, taps):
    local_inputs = voltages.shape[0]
    length = taps.shape[1]
    lags = taps.shape[0]
    spectra_dev = voltages.shape[1] // length
    channels = length // 2
    widen = lax.axis_size("wide")
    ranks = lax.axis_size("tm")
    groups = widen * ranks
    per_group = channels // groups

    tail = voltages[:, (spectra_dev - (lags - 1)) * length :]
    tail = tail.reshape(local_inputs, lags - 1, length).transpose(1, 0, 2).astype(jnp.bfloat16)
    previous = shifted(tail, "tm", 1)
    table = dft_table(length, channels)

    def channelize(filtered):
        return [
            jnp.einsum(
                "sin,nk->kis",
                filtered,
                table[:, part, :],
                precision=lax.Precision.HIGH,
                preferred_element_type=jnp.float32,
            ).astype(jnp.bfloat16)
            for part in range(2)
        ]

    later = channelize(polyphase(voltages, taps, lags - 1, spectra_dev - (lags - 1), None))
    head_frames = voltages[:, : (lags - 1) * length]
    head = channelize(polyphase(head_frames, taps, 0, lags - 1, previous))
    spectra = jnp.concatenate([head[0], later[0], head[1], later[1]], axis=-1)
    packed = spectra.reshape(groups, per_group * local_inputs, 2 * spectra_dev)
    got = lax.all_to_all(packed, ("wide", "tm"), 0, 0, tiled=True)
    got = got.reshape(widen, ranks, per_group * local_inputs, 2 * spectra_dev)
    norm_factor = 1.0 / (spectra_dev * ranks)
    grams = channel_grams(got, norm_factor, per_group)
    back = lax.all_to_all(grams, "tm", 0, 0, tiled=True)
    rows = back.shape[3]
    return back.transpose(3, 1, 0, 2, 4).reshape(rows, 2, ranks * per_group, back.shape[4])


def fir_kernel(first, count, v_ref, taps_ref, *rest):
    if len(rest) == 4:
        h_ref, o_ref, ext_ref, tb_ref = rest
    else:
        h_ref = None
        o_ref, ext_ref, tb_ref = rest
    lags, length = taps_ref.shape
    local_inputs = v_ref.shape[0]
    taps = taps_ref[...].astype(jnp.float32) * FIR_SCALE
    for lag in range(lags):
        tb_ref[lag] = jnp.broadcast_to(taps[lag : lag + 1, :], (local_inputs, length))
    if h_ref is not None:
        ext_ref[0 : lags - 1] = h_ref[...].astype(jnp.float32)

    def fill(j, carry):
        start = pl.multiple_of(j * length, length)
        ext_ref[lags - 1 + j] = v_ref[:, pl.ds(start, length)].astype(jnp.float32)
        return carry

    lax.fori_loop(0, first + count, fill, 0)

    def body(k, carry):
        at = first + k + lags - 1
        acc = tb_ref[0] * ext_ref[at]
        for lag in range(1, lags):
            acc = acc + tb_ref[lag] * ext_ref[at - lag]
        o_ref[k] = acc
        return carry

    lax.fori_loop(0, count, body, 0)


def polyphase(frames, taps, first, count, halo):
    local_inputs = frames.shape[0]
    lags, length = taps.shape
    operands = [frames, taps] + ([halo] if halo is not None else [])
    vmem = pl.BlockSpec(memory_space=pltpu.VMEM)
    return pl.pallas_call(
        lambda *refs: fir_kernel(first, count, *refs),
        out_shape=jax.ShapeDtypeStruct((count, local_inputs, length), jnp.float32),
        in_specs=[vmem] * len(operands),
        out_specs=vmem,
        scratch_shapes=[
            pltpu.VMEM((first + count + lags - 1, local_inputs, length), jnp.float32),
            pltpu.VMEM((lags, local_inputs, length), jnp.float32),
        ],
        cost_estimate=pl.CostEstimate(
            flops=2 * lags * count * local_inputs * length,
            transcendentals=0,
            bytes_accessed=frames.size * 4 + count * local_inputs * length * 4,
        ),
    )(*operands)


def gram_kernel(scale, x_ref, o_ref):
    widen, ranks, stacked, depth = x_ref.shape
    groups = o_ref.shape[2]
    local_inputs = stacked // groups
    inputs = widen * local_inputs
    half = depth // 2
    lane = lax.broadcasted_iota(jnp.int32, (inputs, depth), 1)
    sign = jnp.where(lane < half, -1.0, 1.0).astype(jnp.float32)
    rows = inputs // ranks
    accs = [jnp.zeros((inputs, 2 * inputs), jnp.float32) for _ in range(groups)]
    for t in range(ranks):
        block = x_ref[:, t, :, :].astype(jnp.float32)
        for c in range(groups):
            x = block[:, c * local_inputs : (c + 1) * local_inputs, :].reshape(inputs, depth)
            rot = pltpu.roll(x, half, 1) * sign
            y = jnp.concatenate([x, rot], axis=0).astype(jnp.bfloat16)
            accs[c] = accs[c] + lax.dot_general(
                x.astype(jnp.bfloat16), y, (((1,), (1,)), ((), ())),
                preferred_element_type=jnp.float32,
            )
    for c in range(groups):
        acc = accs[c] * scale
        o_ref[:, 0, c, :, :] = acc[:, :inputs].reshape(ranks, rows, inputs)
        o_ref[:, 1, c, :, :] = acc[:, inputs:].reshape(ranks, rows, inputs)


def channel_grams(got, scale, groups):
    widen, ranks, stacked, depth = got.shape
    inputs = widen * stacked // groups
    rows = inputs // ranks
    flops = 2 * groups * ranks * inputs * 2 * inputs * depth
    return pl.pallas_call(
        lambda x_ref, o_ref: gram_kernel(scale, x_ref, o_ref),
        out_shape=jax.ShapeDtypeStruct((ranks, 2, groups, rows, inputs), jnp.float32),
        in_specs=[pl.BlockSpec(memory_space=pltpu.VMEM)],
        out_specs=pl.BlockSpec(memory_space=pltpu.VMEM),
        cost_estimate=pl.CostEstimate(
            flops=flops, transcendentals=0, bytes_accessed=got.size * 2 + 2 * groups * inputs * inputs * 4
        ),
    )(got)


def solution(mesh):
    placed = (P("wide", "tm"), P())
    return jax.shard_map(
        shards, mesh=mesh, in_specs=placed, out_specs=P("tm", None, "wide", None), check_vma=False
    )
```

```python
import numpy as np
import jax
import jax.numpy as jnp
from jax import lax
from jax.experimental import pallas as pl
from jax.experimental.pallas import tpu as pltpu
from jax.sharding import PartitionSpec as P

FIR_SCALE = 2.0 ** (-12)


def shifted(array, axis, by):
    devices = lax.axis_size(axis)
    pairs = [(i, i + by) for i in range(devices) if 0 <= i + by < devices]
    return lax.ppermute(array, axis, pairs)


def dft_factors(length, channels, split):
    hi = np.arange(length // split)[:, None] * split * np.arange(channels)[None, :] % length
    lo = np.arange(split)[:, None] * np.arange(channels)[None, :] % length
    ang_hi = 2.0 * np.pi / length * hi
    ang_lo = 2.0 * np.pi / length * lo
    return (
        np.cos(ang_hi).astype(np.float32),
        (-np.sin(ang_hi)).astype(np.float32),
        np.cos(ang_lo).astype(np.float32),
        (-np.sin(ang_lo)).astype(np.float32),
    )


def dft_table(length, channels):
    split = 32
    ch, sh, cl, sl = (jnp.asarray(t) for t in dft_factors(length, channels, split))
    re = ch[:, None, :] * cl[None, :, :] - sh[:, None, :] * sl[None, :, :]
    im = ch[:, None, :] * sl[None, :, :] + sh[:, None, :] * cl[None, :, :]
    table = jnp.stack([re, im], axis=2).reshape(length, 2, channels)
    return table * length ** (-0.5)


def shards(voltages, taps):
    local_inputs = voltages.shape[0]
    length = taps.shape[1]
    lags = taps.shape[0]
    spectra_dev = voltages.shape[1] // length
    channels = length // 2
    widen = lax.axis_size("wide")
    ranks = lax.axis_size("tm")
    groups = widen * ranks
    per_group = channels // groups

    frames = voltages.reshape(local_inputs, spectra_dev, length).transpose(1, 0, 2)
    previous = shifted(frames[spectra_dev - (lags - 1) :].astype(jnp.bfloat16), "tm", 1)
    taps_float = taps.astype(jnp.float32)
    table = dft_table(length, channels)

    def channelize(extended, count):
        extended = extended.astype(jnp.float32)
        filtered = taps_float[0] * extended[lags - 1 : lags - 1 + count]
        for lag in range(1, lags):
            filtered = filtered + taps_float[lag] * extended[lags - 1 - lag : lags - 1 - lag + count]
        filtered = filtered * FIR_SCALE
        return [
            jnp.einsum(
                "sin,nk->kis",
                filtered,
                table[:, part, :],
                precision=lax.Precision.HIGH,
                preferred_element_type=jnp.float32,
            ).astype(jnp.bfloat16)
            for part in range(2)
        ]

    later = channelize(frames, spectra_dev - (lags - 1))
    head_frames = [previous.astype(jnp.float32), frames[: 2 * (lags - 1)].astype(jnp.float32)]
    head = channelize(jnp.concatenate(head_frames, axis=0), lags - 1)
    spectra = jnp.concatenate([head[0], later[0], head[1], later[1]], axis=-1)
    packed = spectra.reshape(groups, per_group * local_inputs, 2 * spectra_dev)
    got = lax.all_to_all(packed, ("wide", "tm"), 0, 0, tiled=True)
    got = got.reshape(widen, ranks, per_group * local_inputs, 2 * spectra_dev)
    norm_factor = 1.0 / (spectra_dev * ranks)
    grams = channel_grams(got, norm_factor, per_group)
    back = lax.all_to_all(grams, "tm", 0, 0, tiled=True)
    rows = back.shape[3]
    return back.transpose(3, 1, 0, 2, 4).reshape(rows, 2, ranks * per_group, back.shape[4])


def gram_kernel(scale, x_ref, o_ref):
    widen, ranks, stacked, depth = x_ref.shape
    groups = o_ref.shape[2]
    local_inputs = stacked // groups
    inputs = widen * local_inputs
    half = depth // 2
    lane = lax.broadcasted_iota(jnp.int32, (inputs, depth), 1)
    sign = jnp.where(lane < half, -1.0, 1.0).astype(jnp.float32)
    rows = inputs // ranks
    accs = [jnp.zeros((inputs, 2 * inputs), jnp.float32) for _ in range(groups)]
    for t in range(ranks):
        block = x_ref[:, t, :, :].astype(jnp.float32)
        for c in range(groups):
            x = block[:, c * local_inputs : (c + 1) * local_inputs, :].reshape(inputs, depth)
            rot = pltpu.roll(x, half, 1) * sign
            y = jnp.concatenate([x, rot], axis=0).astype(jnp.bfloat16)
            accs[c] = accs[c] + lax.dot_general(
                x.astype(jnp.bfloat16), y, (((1,), (1,)), ((), ())),
                preferred_element_type=jnp.float32,
            )
    for c in range(groups):
        acc = accs[c] * scale
        o_ref[:, 0, c, :, :] = acc[:, :inputs].reshape(ranks, rows, inputs)
        o_ref[:, 1, c, :, :] = acc[:, inputs:].reshape(ranks, rows, inputs)


def channel_grams(got, scale, groups):
    widen, ranks, stacked, depth = got.shape
    inputs = widen * stacked // groups
    rows = inputs // ranks
    flops = 2 * groups * ranks * inputs * 2 * inputs * depth
    return pl.pallas_call(
        lambda x_ref, o_ref: gram_kernel(scale, x_ref, o_ref),
        out_shape=jax.ShapeDtypeStruct((ranks, 2, groups, rows, inputs), jnp.float32),
        in_specs=[pl.BlockSpec(memory_space=pltpu.VMEM)],
        out_specs=pl.BlockSpec(memory_space=pltpu.VMEM),
        cost_estimate=pl.CostEstimate(
            flops=flops, transcendentals=0, bytes_accessed=got.size * 2 + 2 * groups * inputs * inputs * 4
        ),
    )(got)


def solution(mesh):
    placed = (P("wide", "tm"), P())
    return jax.shard_map(
        shards, mesh=mesh, in_specs=placed, out_specs=P("tm", None, "wide", None), check_vma=False
    )
```

```python
import numpy as np
import jax
import jax.numpy as jnp
from jax import lax
from jax.experimental import pallas as pl
from jax.experimental.pallas import tpu as pltpu
from jax.sharding import PartitionSpec as P

FIR_SCALE = 2.0 ** (-12)


def shifted(array, axis, by):
    devices = lax.axis_size(axis)
    pairs = [(i, i + by) for i in range(devices) if 0 <= i + by < devices]
    return lax.ppermute(array, axis, pairs)


def dft_factors(length, channels, split):
    hi = np.arange(length // split)[:, None] * split * np.arange(channels)[None, :] % length
    lo = np.arange(split)[:, None] * np.arange(channels)[None, :] % length
    ang_hi = 2.0 * np.pi / length * hi
    ang_lo = 2.0 * np.pi / length * lo
    return (
        np.cos(ang_hi).astype(np.float32),
        (-np.sin(ang_hi)).astype(np.float32),
        np.cos(ang_lo).astype(np.float32),
        (-np.sin(ang_lo)).astype(np.float32),
    )


def dft_table(length, channels):
    split = 32
    ch, sh, cl, sl = (jnp.asarray(t) for t in dft_factors(length, channels, split))
    re = ch[:, None, :] * cl[None, :, :] - sh[:, None, :] * sl[None, :, :]
    im = ch[:, None, :] * sl[None, :, :] + sh[:, None, :] * cl[None, :, :]
    table = jnp.stack([re, im], axis=2).reshape(length, 2, channels)
    return table * length ** (-0.5)


def shards(voltages, taps):
    local_inputs = voltages.shape[0]
    length = taps.shape[1]
    lags = taps.shape[0]
    spectra_dev = voltages.shape[1] // length
    channels = length // 2
    widen = lax.axis_size("wide")
    ranks = lax.axis_size("tm")
    groups = widen * ranks
    per_group = channels // groups

    frames = voltages.reshape(local_inputs, spectra_dev, length).transpose(1, 0, 2)
    previous = shifted(frames[spectra_dev - (lags - 1) :].astype(jnp.bfloat16), "tm", 1)
    taps_float = taps.astype(jnp.float32)
    table = dft_table(length, channels)

    def channelize(extended, count):
        extended = extended.astype(jnp.float32)
        filtered = taps_float[0] * extended[lags - 1 : lags - 1 + count]
        for lag in range(1, lags):
            filtered = filtered + taps_float[lag] * extended[lags - 1 - lag : lags - 1 - lag + count]
        filtered = filtered * FIR_SCALE
        return [
            jnp.einsum(
                "sin,nk->sik",
                filtered,
                table[:, part, :],
                precision=lax.Precision.HIGH,
                preferred_element_type=jnp.float32,
            ).astype(jnp.bfloat16)
            for part in range(2)
        ]

    later = channelize(frames, spectra_dev - (lags - 1))
    head_frames = [previous.astype(jnp.float32), frames[: 2 * (lags - 1)].astype(jnp.float32)]
    head = channelize(jnp.concatenate(head_frames, axis=0), lags - 1)
    pieces = [head[0], later[0], head[1], later[1]]
    spectra = jnp.concatenate([piece.transpose(2, 1, 0) for piece in pieces], axis=-1)
    packed = spectra.reshape(groups, per_group * local_inputs, 2 * spectra_dev)
    got = lax.all_to_all(packed, ("wide", "tm"), 0, 0, tiled=True)
    got = got.reshape(widen, ranks, per_group * local_inputs, 2 * spectra_dev)
    norm_factor = 1.0 / (spectra_dev * ranks)
    grams = channel_grams(got, norm_factor, per_group)
    back = lax.all_to_all(grams, "tm", 0, 0, tiled=True)
    rows = back.shape[3]
    return back.transpose(3, 1, 0, 2, 4).reshape(rows, 2, ranks * per_group, back.shape[4])


def gram_kernel(scale, x_ref, o_ref):
    widen, ranks, stacked, depth = x_ref.shape
    groups = o_ref.shape[2]
    local_inputs = stacked // groups
    inputs = widen * local_inputs
    half = depth // 2
    lane = lax.broadcasted_iota(jnp.int32, (inputs, depth), 1)
    sign = jnp.where(lane < half, -1.0, 1.0).astype(jnp.float32)
    rows = inputs // ranks
    accs = [jnp.zeros((inputs, 2 * inputs), jnp.float32) for _ in range(groups)]
    for t in range(ranks):
        block = x_ref[:, t, :, :].astype(jnp.float32)
        for c in range(groups):
            x = block[:, c * local_inputs : (c + 1) * local_inputs, :].reshape(inputs, depth)
            rot = pltpu.roll(x, half, 1) * sign
            y = jnp.concatenate([x, rot], axis=0).astype(jnp.bfloat16)
            accs[c] = accs[c] + lax.dot_general(
                x.astype(jnp.bfloat16), y, (((1,), (1,)), ((), ())),
                preferred_element_type=jnp.float32,
            )
    for c in range(groups):
        acc = accs[c] * scale
        o_ref[:, 0, c, :, :] = acc[:, :inputs].reshape(ranks, rows, inputs)
        o_ref[:, 1, c, :, :] = acc[:, inputs:].reshape(ranks, rows, inputs)


def channel_grams(got, scale, groups):
    widen, ranks, stacked, depth = got.shape
    inputs = widen * stacked // groups
    rows = inputs // ranks
    flops = 2 * groups * ranks * inputs * 2 * inputs * depth
    return pl.pallas_call(
        lambda x_ref, o_ref: gram_kernel(scale, x_ref, o_ref),
        out_shape=jax.ShapeDtypeStruct((ranks, 2, groups, rows, inputs), jnp.float32),
        in_specs=[pl.BlockSpec(memory_space=pltpu.VMEM)],
        out_specs=pl.BlockSpec(memory_space=pltpu.VMEM),
        cost_estimate=pl.CostEstimate(
            flops=flops, transcendentals=0, bytes_accessed=got.size * 2 + 2 * groups * inputs * inputs * 4
        ),
    )(got)


def solution(mesh):
    placed = (P("wide", "tm"), P())
    return jax.shard_map(
        shards, mesh=mesh, in_specs=placed, out_specs=P("tm", None, "wide", None), check_vma=False
    )
```

```python
import numpy as np
import jax
import jax.numpy as jnp
from jax import lax
from jax.experimental import pallas as pl
from jax.experimental.pallas import tpu as pltpu
from jax.sharding import PartitionSpec as P

FIR_SCALE = 2.0 ** (-12)


def shifted(array, axis, by):
    devices = lax.axis_size(axis)
    pairs = [(i, i + by) for i in range(devices) if 0 <= i + by < devices]
    return lax.ppermute(array, axis, pairs)


def radix4_tables(length, channels):
    quarter = length // 4
    n0 = np.arange(quarter)[:, None]
    scale = length ** (-0.5)

    def parts(q):
        k = 4 * np.arange(channels // 4)[None, :] + q
        angle = 2.0 * np.pi / length * (n0 * k % length)
        return np.cos(angle) * scale, np.sin(angle) * scale

    c0, s0 = parts(0)
    c1, s1 = parts(1)
    c2, s2 = parts(2)
    c3, s3 = parts(3)
    real_q0 = np.concatenate([c0, -s0], axis=1)
    real_q2 = np.concatenate([c2, -s2], axis=1)
    mixed = np.block([[c1, -s1, c3, -s3], [-s1, -c1, s3, c3]])
    return tuple(t.astype(np.float32) for t in (real_q0, real_q2, mixed))


def shards(voltages, taps):
    local_inputs = voltages.shape[0]
    length = taps.shape[1]
    lags = taps.shape[0]
    spectra_dev = voltages.shape[1] // length
    channels = length // 2
    widen = lax.axis_size("wide")
    ranks = lax.axis_size("tm")
    groups = widen * ranks
    per_group = channels // groups

    frames = voltages.reshape(local_inputs, spectra_dev, length).transpose(1, 0, 2)
    frames = frames.astype(jnp.bfloat16)
    previous = shifted(frames[spectra_dev - (lags - 1) :], "tm", 1)
    taps_float = taps.astype(jnp.float32)
    tables = [jnp.asarray(t) for t in radix4_tables(length, channels)]
    quarter = length // 4

    def channelize(extended, count):
        extended = extended.astype(jnp.float32)
        filtered = taps_float[0] * extended[lags - 1 : lags - 1 + count]
        for lag in range(1, lags):
            filtered = filtered + taps_float[lag] * extended[lags - 1 - lag : lags - 1 - lag + count]
        filtered = filtered * FIR_SCALE
        x0, x1, x2, x3 = (filtered[..., m * quarter : (m + 1) * quarter] for m in range(4))
        inputs = [x0 + x1 + x2 + x3, x0 - x1 + x2 - x3, jnp.concatenate([x0 - x2, x1 - x3], axis=-1)]
        outs = [
            jnp.einsum(
                "sin,nm->sim",
                lhs,
                table,
                precision=lax.Precision.HIGH,
                preferred_element_type=jnp.float32,
            ).astype(jnp.bfloat16)
            for lhs, table in zip(inputs, tables)
        ]
        per_q = channels // 4
        q0, q2, q13 = outs
        real = jnp.stack([q0[..., :per_q], q13[..., :per_q], q2[..., :per_q], q13[..., 2 * per_q : 3 * per_q]], axis=2)
        imag = jnp.stack([q0[..., per_q:], q13[..., per_q : 2 * per_q], q2[..., per_q:], q13[..., 3 * per_q :]], axis=2)
        return [part.transpose(3, 2, 1, 0).reshape(channels, local_inputs, count) for part in (real, imag)]

    later = channelize(frames, spectra_dev - (lags - 1))
    head = channelize(jnp.concatenate([previous, frames[: 2 * (lags - 1)]], axis=0), lags - 1)
    spectra = jnp.concatenate([head[0], later[0], head[1], later[1]], axis=-1)
    packed = spectra.reshape(groups, per_group * local_inputs, 2 * spectra_dev)
    got = lax.all_to_all(packed, ("wide", "tm"), 0, 0, tiled=True)
    got = got.reshape(widen, ranks, per_group * local_inputs, 2 * spectra_dev)
    norm_factor = 1.0 / (spectra_dev * ranks)
    grams = channel_grams(got, norm_factor, per_group)
    back = lax.all_to_all(grams, "tm", 0, 0, tiled=True)
    rows = back.shape[3]
    return back.transpose(3, 1, 0, 2, 4).reshape(rows, 2, ranks * per_group, back.shape[4])


def gram_kernel(scale, x_ref, o_ref):
    widen, ranks, stacked, depth = x_ref.shape
    groups = o_ref.shape[2]
    local_inputs = stacked // groups
    inputs = widen * local_inputs
    half = depth // 2
    lane = lax.broadcasted_iota(jnp.int32, (inputs, depth), 1)
    sign = jnp.where(lane < half, -1.0, 1.0).astype(jnp.float32)
    rows = inputs // ranks
    accs = [jnp.zeros((inputs, 2 * inputs), jnp.float32) for _ in range(groups)]
    for t in range(ranks):
        block = x_ref[:, t, :, :].astype(jnp.float32)
        for c in range(groups):
            x = block[:, c * local_inputs : (c + 1) * local_inputs, :].reshape(inputs, depth)
            rot = pltpu.roll(x, half, 1) * sign
            y = jnp.concatenate([x, rot], axis=0).astype(jnp.bfloat16)
            accs[c] = accs[c] + lax.dot_general(
                x.astype(jnp.bfloat16), y, (((1,), (1,)), ((), ())),
                preferred_element_type=jnp.float32,
            )
    for c in range(groups):
        acc = accs[c] * scale
        o_ref[:, 0, c, :, :] = acc[:, :inputs].reshape(ranks, rows, inputs)
        o_ref[:, 1, c, :, :] = acc[:, inputs:].reshape(ranks, rows, inputs)


def channel_grams(got, scale, groups):
    widen, ranks, stacked, depth = got.shape
    inputs = widen * stacked // groups
    rows = inputs // ranks
    flops = 2 * groups * ranks * inputs * 2 * inputs * depth
    return pl.pallas_call(
        lambda x_ref, o_ref: gram_kernel(scale, x_ref, o_ref),
        out_shape=jax.ShapeDtypeStruct((ranks, 2, groups, rows, inputs), jnp.float32),
        in_specs=[pl.BlockSpec(memory_space=pltpu.VMEM)],
        out_specs=pl.BlockSpec(memory_space=pltpu.VMEM),
        cost_estimate=pl.CostEstimate(
            flops=flops, transcendentals=0, bytes_accessed=got.size * 2 + 2 * groups * inputs * inputs * 4
        ),
    )(got)


def solution(mesh):
    placed = (P("wide", "tm"), P())
    return jax.shard_map(
        shards, mesh=mesh, in_specs=placed, out_specs=P("tm", None, "wide", None), check_vma=False
    )
```

```python
import numpy as np
import jax
import jax.numpy as jnp
from jax import lax
from jax.experimental import pallas as pl
from jax.experimental.pallas import tpu as pltpu
from jax.sharding import PartitionSpec as P

FIR_SCALE = 2.0 ** (-12)


def shifted(array, axis, by):
    devices = lax.axis_size(axis)
    pairs = [(i, i + by) for i in range(devices) if 0 <= i + by < devices]
    return lax.ppermute(array, axis, pairs)


def radix4_tables(length, channels):
    quarter = length // 4
    n0 = np.arange(quarter)[:, None]
    scale = length ** (-0.5)

    def parts(q):
        k = 4 * np.arange(channels // 4)[None, :] + q
        angle = 2.0 * np.pi / length * (n0 * k % length)
        return np.cos(angle) * scale, np.sin(angle) * scale

    c0, s0 = parts(0)
    c1, s1 = parts(1)
    c2, s2 = parts(2)
    c3, s3 = parts(3)
    zero = np.zeros_like(c0)
    even = np.block([[c0, -s0, zero, zero], [zero, zero, c2, -s2]])
    odd = np.block([[c1, -s1, c3, -s3], [-s1, -c1, s3, c3]])
    return tuple(t.astype(np.float32) for t in (even, odd))


def shards(voltages, taps):
    local_inputs = voltages.shape[0]
    length = taps.shape[1]
    lags = taps.shape[0]
    spectra_dev = voltages.shape[1] // length
    channels = length // 2
    widen = lax.axis_size("wide")
    ranks = lax.axis_size("tm")
    groups = widen * ranks
    per_group = channels // groups

    frames = voltages.reshape(local_inputs, spectra_dev, length).transpose(1, 0, 2)
    frames = frames.astype(jnp.bfloat16)
    previous = shifted(frames[spectra_dev - (lags - 1) :], "tm", 1)
    taps_float = taps.astype(jnp.float32)
    tables = [jnp.asarray(t) for t in radix4_tables(length, channels)]
    quarter = length // 4

    def channelize(extended, count):
        extended = extended.astype(jnp.float32)
        filtered = taps_float[0] * extended[lags - 1 : lags - 1 + count]
        for lag in range(1, lags):
            filtered = filtered + taps_float[lag] * extended[lags - 1 - lag : lags - 1 - lag + count]
        filtered = filtered * FIR_SCALE
        x0, x1, x2, x3 = (filtered[..., m * quarter : (m + 1) * quarter] for m in range(4))
        inputs = [
            jnp.concatenate([x0 + x1 + x2 + x3, x0 - x1 + x2 - x3], axis=-1),
            jnp.concatenate([x0 - x2, x1 - x3], axis=-1),
        ]
        even, odd = (
            jnp.einsum(
                "sin,nm->sim",
                lhs,
                table,
                precision=lax.Precision.HIGH,
                preferred_element_type=jnp.float32,
            )
            .astype(jnp.bfloat16)
            .reshape(count, local_inputs, 2, 2, channels // 4)
            for lhs, table in zip(inputs, tables)
        )
        return jnp.stack([even[:, :, 0], odd[:, :, 0], even[:, :, 1], odd[:, :, 1]], axis=2)

    later = channelize(frames, spectra_dev - (lags - 1))
    head = channelize(jnp.concatenate([previous, frames[: 2 * (lags - 1)]], axis=0), lags - 1)
    spectra = jnp.concatenate([head, later], axis=0).transpose(4, 2, 1, 3, 0)
    spectra = spectra.reshape(channels, local_inputs, 2 * spectra_dev)
    packed = spectra.reshape(groups, per_group * local_inputs, 2 * spectra_dev)
    got = lax.all_to_all(packed, ("wide", "tm"), 0, 0, tiled=True)
    got = got.reshape(widen, ranks, per_group * local_inputs, 2 * spectra_dev)
    norm_factor = 1.0 / (spectra_dev * ranks)
    grams = channel_grams(got, norm_factor, per_group)
    back = lax.all_to_all(grams, "tm", 0, 0, tiled=True)
    rows = back.shape[3]
    return back.transpose(3, 1, 0, 2, 4).reshape(rows, 2, ranks * per_group, back.shape[4])


def gram_kernel(scale, x_ref, o_ref):
    widen, ranks, stacked, depth = x_ref.shape
    groups = o_ref.shape[2]
    local_inputs = stacked // groups
    inputs = widen * local_inputs
    half = depth // 2
    lane = lax.broadcasted_iota(jnp.int32, (inputs, depth), 1)
    sign = jnp.where(lane < half, -1.0, 1.0).astype(jnp.float32)
    rows = inputs // ranks
    accs = [jnp.zeros((inputs, 2 * inputs), jnp.float32) for _ in range(groups)]
    for t in range(ranks):
        block = x_ref[:, t, :, :].astype(jnp.float32)
        for c in range(groups):
            x = block[:, c * local_inputs : (c + 1) * local_inputs, :].reshape(inputs, depth)
            rot = pltpu.roll(x, half, 1) * sign
            y = jnp.concatenate([x, rot], axis=0).astype(jnp.bfloat16)
            accs[c] = accs[c] + lax.dot_general(
                x.astype(jnp.bfloat16), y, (((1,), (1,)), ((), ())),
                preferred_element_type=jnp.float32,
            )
    for c in range(groups):
        acc = accs[c] * scale
        o_ref[:, 0, c, :, :] = acc[:, :inputs].reshape(ranks, rows, inputs)
        o_ref[:, 1, c, :, :] = acc[:, inputs:].reshape(ranks, rows, inputs)


def channel_grams(got, scale, groups):
    widen, ranks, stacked, depth = got.shape
    inputs = widen * stacked // groups
    rows = inputs // ranks
    flops = 2 * groups * ranks * inputs * 2 * inputs * depth
    return pl.pallas_call(
        lambda x_ref, o_ref: gram_kernel(scale, x_ref, o_ref),
        out_shape=jax.ShapeDtypeStruct((ranks, 2, groups, rows, inputs), jnp.float32),
        in_specs=[pl.BlockSpec(memory_space=pltpu.VMEM)],
        out_specs=pl.BlockSpec(memory_space=pltpu.VMEM),
        cost_estimate=pl.CostEstimate(
            flops=flops, transcendentals=0, bytes_accessed=got.size * 2 + 2 * groups * inputs * inputs * 4
        ),
    )(got)


def solution(mesh):
    placed = (P("wide", "tm"), P())
    return jax.shard_map(
        shards, mesh=mesh, in_specs=placed, out_specs=P("tm", None, "wide", None), check_vma=False
    )
```

```python
import numpy as np
import jax
import jax.numpy as jnp
from jax import lax
from jax.experimental import pallas as pl
from jax.experimental.pallas import tpu as pltpu
from jax.sharding import PartitionSpec as P

FIR_SCALE = 2.0 ** (-12)


def shifted(array, axis, by):
    devices = lax.axis_size(axis)
    pairs = [(i, i + by) for i in range(devices) if 0 <= i + by < devices]
    return lax.ppermute(array, axis, pairs)


def radix4_tables(length, channels):
    quarter = length // 4
    n0 = np.arange(quarter)[:, None]
    scale = length ** (-0.5)

    def parts(q):
        k = 4 * np.arange(channels // 4)[None, :] + q
        angle = 2.0 * np.pi / length * (n0 * k % length)
        return np.cos(angle) * scale, np.sin(angle) * scale

    c0, s0 = parts(0)
    c1, s1 = parts(1)
    c2, s2 = parts(2)
    c3, s3 = parts(3)
    zero = np.zeros_like(c0)
    even = np.block([[c0, -s0, zero, zero], [zero, zero, c2, -s2]])
    odd = np.block([[c1, -s1, c3, -s3], [-s1, -c1, s3, c3]])
    return tuple(t.astype(np.float32) for t in (even, odd))


def shards(voltages, taps):
    local_inputs = voltages.shape[0]
    length = taps.shape[1]
    lags = taps.shape[0]
    spectra_dev = voltages.shape[1] // length
    channels = length // 2
    widen = lax.axis_size("wide")
    ranks = lax.axis_size("tm")
    groups = widen * ranks
    per_group = channels // groups

    frames = voltages.reshape(local_inputs, spectra_dev, length).transpose(1, 0, 2)
    frames = frames.astype(jnp.bfloat16)
    previous = shifted(frames[spectra_dev - (lags - 1) :], "tm", 1)
    taps_float = taps.astype(jnp.float32)
    tables = [jnp.asarray(t) for t in radix4_tables(length, channels)]
    quarter = length // 4

    def channelize(extended, count):
        extended = extended.astype(jnp.float32)
        filtered = taps_float[0] * extended[lags - 1 : lags - 1 + count]
        for lag in range(1, lags):
            filtered = filtered + taps_float[lag] * extended[lags - 1 - lag : lags - 1 - lag + count]
        filtered = filtered * FIR_SCALE
        x0, x1, x2, x3 = (filtered[..., m * quarter : (m + 1) * quarter] for m in range(4))
        inputs = [
            jnp.concatenate([x0 + x1 + x2 + x3, x0 - x1 + x2 - x3], axis=-1),
            jnp.concatenate([x0 - x2, x1 - x3], axis=-1),
        ]
        even, odd = (
            jnp.einsum(
                "sin,nm->sim",
                lhs,
                table,
                precision=lax.Precision.HIGH,
                preferred_element_type=jnp.float32,
            )
            .astype(jnp.bfloat16)
            .reshape(count, local_inputs, 2, 2, channels // 4)
            for lhs, table in zip(inputs, tables)
        )
        return jnp.stack([even[:, :, 0], odd[:, :, 0], even[:, :, 1], odd[:, :, 1]], axis=2)

    later = channelize(frames, spectra_dev - (lags - 1))
    head = channelize(jnp.concatenate([previous, frames[: 2 * (lags - 1)]], axis=0), lags - 1)
    spectra = jnp.concatenate([head, later], axis=0).transpose(4, 2, 1, 3, 0)
    spectra = spectra.reshape(channels, local_inputs, 2 * spectra_dev)
    packed = spectra.reshape(groups, per_group * local_inputs, 2 * spectra_dev)
    got = lax.all_to_all(packed, ("wide", "tm"), 0, 0, tiled=True)
    got = got.reshape(widen, ranks, per_group * local_inputs, 2 * spectra_dev)
    norm_factor = 1.0 / (spectra_dev * ranks)
    grams = channel_grams(got, norm_factor, per_group)
    back = lax.all_to_all(grams, "tm", 0, 0, tiled=True)
    rows = back.shape[3]
    return back.transpose(3, 1, 0, 2, 4).reshape(rows, 2, ranks * per_group, back.shape[4])


def gram_kernel(scale, x_ref, o_ref, acc_ref):
    t = pl.program_id(0)
    widen, _, stacked, depth = x_ref.shape
    ranks, _, groups, rows, inputs = o_ref.shape
    local_inputs = stacked // groups
    half = depth // 2
    lane = lax.broadcasted_iota(jnp.int32, (inputs, depth), 1)
    sign = jnp.where(lane < half, -1.0, 1.0).astype(jnp.float32)

    @pl.when(t == 0)
    def _():
        acc_ref[...] = jnp.zeros_like(acc_ref)

    block = x_ref[:, 0, :, :].astype(jnp.float32)
    for c in range(groups):
        x = block[:, c * local_inputs : (c + 1) * local_inputs, :].reshape(inputs, depth)
        rot = pltpu.roll(x, half, 1) * sign
        y = jnp.concatenate([x, rot], axis=0).astype(jnp.bfloat16)
        acc_ref[c] += lax.dot_general(
            x.astype(jnp.bfloat16), y, (((1,), (1,)), ((), ())),
            preferred_element_type=jnp.float32,
        )

    @pl.when(t == ranks - 1)
    def _():
        for c in range(groups):
            acc = acc_ref[c] * scale
            o_ref[:, 0, c, :, :] = acc[:, :inputs].reshape(ranks, rows, inputs)
            o_ref[:, 1, c, :, :] = acc[:, inputs:].reshape(ranks, rows, inputs)


def channel_grams(got, scale, groups):
    widen, ranks, stacked, depth = got.shape
    inputs = widen * stacked // groups
    rows = inputs // ranks
    flops = 2 * groups * ranks * inputs * 2 * inputs * depth
    return pl.pallas_call(
        lambda x_ref, o_ref, acc_ref: gram_kernel(scale, x_ref, o_ref, acc_ref),
        out_shape=jax.ShapeDtypeStruct((ranks, 2, groups, rows, inputs), jnp.float32),
        grid=(ranks,),
        in_specs=[pl.BlockSpec((widen, 1, stacked, depth), lambda t: (0, t, 0, 0))],
        out_specs=pl.BlockSpec((ranks, 2, groups, rows, inputs), lambda t: (0, 0, 0, 0, 0)),
        scratch_shapes=[pltpu.VMEM((groups, inputs, 2 * inputs), jnp.float32)],
        compiler_params=pltpu.CompilerParams(dimension_semantics=("arbitrary",)),
        cost_estimate=pl.CostEstimate(
            flops=flops, transcendentals=0, bytes_accessed=got.size * 2 + 2 * groups * inputs * inputs * 4
        ),
    )(got)


def solution(mesh):
    placed = (P("wide", "tm"), P())
    return jax.shard_map(
        shards, mesh=mesh, in_specs=placed, out_specs=P("tm", None, "wide", None), check_vma=False
    )
```

```python
import numpy as np
import jax
import jax.numpy as jnp
from jax import lax
from jax.experimental import pallas as pl
from jax.experimental.pallas import tpu as pltpu
from jax.sharding import PartitionSpec as P

FIR_SCALE = 2.0 ** (-12)


def shifted(array, axis, by):
    devices = lax.axis_size(axis)
    pairs = [(i, i + by) for i in range(devices) if 0 <= i + by < devices]
    return lax.ppermute(array, axis, pairs)


def radix4_factors(length, channels, split):
    quarter = length // 4
    k = (4 * np.arange(channels // 4)[None, :] + np.arange(4)[:, None]).reshape(1, channels)
    hi = np.arange(quarter // split)[:, None] * split * k % length
    lo = np.arange(split)[:, None] * k % length
    angles = [2.0 * np.pi / length * hi, 2.0 * np.pi / length * lo]
    return [f(angle).astype(np.float32) for angle in angles for f in (np.cos, np.sin)]


def radix4_tables(length, channels):
    split = 16
    ch, sh, cl, sl = (jnp.asarray(t) for t in radix4_factors(length, channels, split))
    quarter = length // 4
    cos = (ch[:, None, :] * cl[None, :, :] - sh[:, None, :] * sl[None, :, :]).reshape(quarter, channels)
    sin = (sh[:, None, :] * cl[None, :, :] + ch[:, None, :] * sl[None, :, :]).reshape(quarter, channels)
    cos = cos * length ** (-0.5)
    sin = sin * length ** (-0.5)
    per_q = channels // 4
    c0, c1, c2, c3 = (cos[:, q * per_q : (q + 1) * per_q] for q in range(4))
    s0, s1, s2, s3 = (sin[:, q * per_q : (q + 1) * per_q] for q in range(4))
    zero = jnp.zeros_like(c0)
    even = jnp.block([[c0, -s0, zero, zero], [zero, zero, c2, -s2]])
    odd = jnp.block([[c1, -s1, c3, -s3], [-s1, -c1, s3, c3]])
    return even, odd


def shards(voltages, taps):
    local_inputs = voltages.shape[0]
    length = taps.shape[1]
    lags = taps.shape[0]
    spectra_dev = voltages.shape[1] // length
    channels = length // 2
    widen = lax.axis_size("wide")
    ranks = lax.axis_size("tm")
    groups = widen * ranks
    per_group = channels // groups

    frames = voltages.reshape(local_inputs, spectra_dev, length).transpose(1, 0, 2)
    frames = frames.astype(jnp.bfloat16)
    previous = shifted(frames[spectra_dev - (lags - 1) :], "tm", 1)
    taps_float = taps.astype(jnp.float32)
    tables = radix4_tables(length, channels)
    quarter = length // 4

    def channelize(extended, count):
        extended = extended.astype(jnp.float32)
        filtered = taps_float[0] * extended[lags - 1 : lags - 1 + count]
        for lag in range(1, lags):
            filtered = filtered + taps_float[lag] * extended[lags - 1 - lag : lags - 1 - lag + count]
        filtered = filtered * FIR_SCALE
        x0, x1, x2, x3 = (filtered[..., m * quarter : (m + 1) * quarter] for m in range(4))
        inputs = [
            jnp.concatenate([x0 + x1 + x2 + x3, x0 - x1 + x2 - x3], axis=-1),
            jnp.concatenate([x0 - x2, x1 - x3], axis=-1),
        ]
        even, odd = (
            jnp.einsum(
                "sin,nm->sim",
                lhs,
                table,
                precision=lax.Precision.HIGH,
                preferred_element_type=jnp.float32,
            )
            .astype(jnp.bfloat16)
            .reshape(count, local_inputs, 2, 2, channels // 4)
            for lhs, table in zip(inputs, tables)
        )
        return jnp.stack([even[:, :, 0], odd[:, :, 0], even[:, :, 1], odd[:, :, 1]], axis=2)

    later = channelize(frames, spectra_dev - (lags - 1))
    head = channelize(jnp.concatenate([previous, frames[: 2 * (lags - 1)]], axis=0), lags - 1)
    spectra = jnp.concatenate([head, later], axis=0).transpose(4, 2, 1, 3, 0)
    spectra = spectra.reshape(channels, local_inputs, 2 * spectra_dev)
    packed = spectra.reshape(groups, per_group * local_inputs, 2 * spectra_dev)
    got = lax.all_to_all(packed, ("wide", "tm"), 0, 0, tiled=True)
    got = got.reshape(widen, ranks, per_group * local_inputs, 2 * spectra_dev)
    norm_factor = 1.0 / (spectra_dev * ranks)
    grams = channel_grams(got, norm_factor, per_group)
    back = lax.all_to_all(grams, "tm", 0, 0, tiled=True)
    rows = back.shape[3]
    return back.transpose(3, 1, 0, 2, 4).reshape(rows, 2, ranks * per_group, back.shape[4])


def gram_kernel(scale, x_ref, o_ref):
    widen, ranks, stacked, depth = x_ref.shape
    groups = o_ref.shape[2]
    local_inputs = stacked // groups
    inputs = widen * local_inputs
    half = depth // 2
    lane = lax.broadcasted_iota(jnp.int32, (inputs, depth), 1)
    sign = jnp.where(lane < half, -1.0, 1.0).astype(jnp.float32)
    rows = inputs // ranks
    accs = [jnp.zeros((inputs, 2 * inputs), jnp.float32) for _ in range(groups)]
    for t in range(ranks):
        block = x_ref[:, t, :, :].astype(jnp.float32)
        for c in range(groups):
            x = block[:, c * local_inputs : (c + 1) * local_inputs, :].reshape(inputs, depth)
            rot = pltpu.roll(x, half, 1) * sign
            y = jnp.concatenate([x, rot], axis=0).astype(jnp.bfloat16)
            accs[c] = accs[c] + lax.dot_general(
                x.astype(jnp.bfloat16), y, (((1,), (1,)), ((), ())),
                preferred_element_type=jnp.float32,
            )
    for c in range(groups):
        acc = accs[c] * scale
        o_ref[:, 0, c, :, :] = acc[:, :inputs].reshape(ranks, rows, inputs)
        o_ref[:, 1, c, :, :] = acc[:, inputs:].reshape(ranks, rows, inputs)


def channel_grams(got, scale, groups):
    widen, ranks, stacked, depth = got.shape
    inputs = widen * stacked // groups
    rows = inputs // ranks
    flops = 2 * groups * ranks * inputs * 2 * inputs * depth
    return pl.pallas_call(
        lambda x_ref, o_ref: gram_kernel(scale, x_ref, o_ref),
        out_shape=jax.ShapeDtypeStruct((ranks, 2, groups, rows, inputs), jnp.float32),
        in_specs=[pl.BlockSpec(memory_space=pltpu.VMEM)],
        out_specs=pl.BlockSpec(memory_space=pltpu.VMEM),
        cost_estimate=pl.CostEstimate(
            flops=flops, transcendentals=0, bytes_accessed=got.size * 2 + 2 * groups * inputs * inputs * 4
        ),
    )(got)


def solution(mesh):
    placed = (P("wide", "tm"), P())
    return jax.shard_map(
        shards, mesh=mesh, in_specs=placed, out_specs=P("tm", None, "wide", None), check_vma=False
    )
```

```python
import numpy as np
import jax
import jax.numpy as jnp
from jax import lax
from jax.experimental import pallas as pl
from jax.experimental.pallas import tpu as pltpu
from jax.sharding import PartitionSpec as P

FIR_SCALE = 2.0 ** (-12)


def shifted(array, axis, by):
    devices = lax.axis_size(axis)
    pairs = [(i, i + by) for i in range(devices) if 0 <= i + by < devices]
    return lax.ppermute(array, axis, pairs)


def radix4_factors(length, channels, split):
    quarter = length // 4
    k = (4 * np.arange(channels // 4)[None, :] + np.arange(4)[:, None]).reshape(1, channels)
    hi = np.arange(quarter // split)[:, None] * split * k % length
    lo = np.arange(split)[:, None] * k % length
    angles = [2.0 * np.pi / length * hi, 2.0 * np.pi / length * lo]
    return [f(angle).astype(np.float32) for angle in angles for f in (np.cos, np.sin)]


def radix4_tables(length, channels):
    split = 16
    ch, sh, cl, sl = (jnp.asarray(t) for t in radix4_factors(length, channels, split))
    quarter = length // 4
    cos = (ch[:, None, :] * cl[None, :, :] - sh[:, None, :] * sl[None, :, :]).reshape(quarter, channels)
    sin = (sh[:, None, :] * cl[None, :, :] + ch[:, None, :] * sl[None, :, :]).reshape(quarter, channels)
    cos = cos * length ** (-0.5)
    sin = sin * length ** (-0.5)
    per_q = channels // 4
    c0, c1, c2, c3 = (cos[:, q * per_q : (q + 1) * per_q] for q in range(4))
    s0, s1, s2, s3 = (sin[:, q * per_q : (q + 1) * per_q] for q in range(4))
    real_q0 = jnp.concatenate([c0, -s0], axis=1)
    real_q2 = jnp.concatenate([c2, -s2], axis=1)
    odd = jnp.block([[c1, -s1, c3, -s3], [-s1, -c1, s3, c3]])
    return real_q0, real_q2, odd


def shards(voltages, taps):
    local_inputs = voltages.shape[0]
    length = taps.shape[1]
    lags = taps.shape[0]
    spectra_dev = voltages.shape[1] // length
    channels = length // 2
    widen = lax.axis_size("wide")
    ranks = lax.axis_size("tm")
    groups = widen * ranks
    per_group = channels // groups

    frames = voltages.reshape(local_inputs, spectra_dev, length).transpose(1, 0, 2)
    frames = frames.astype(jnp.bfloat16)
    previous = shifted(frames[spectra_dev - (lags - 1) :], "tm", 1)
    taps_float = taps.astype(jnp.float32)
    tables = radix4_tables(length, channels)
    quarter = length // 4

    def channelize(extended, count):
        extended = extended.astype(jnp.float32)
        filtered = taps_float[0] * extended[lags - 1 : lags - 1 + count]
        for lag in range(1, lags):
            filtered = filtered + taps_float[lag] * extended[lags - 1 - lag : lags - 1 - lag + count]
        filtered = filtered * FIR_SCALE
        x0, x1, x2, x3 = (filtered[..., m * quarter : (m + 1) * quarter] for m in range(4))
        def dft(lhs, table):
            return jnp.einsum(
                "sin,nm->sim",
                lhs,
                table,
                precision=lax.Precision.HIGH,
                preferred_element_type=jnp.float32,
            ).astype(jnp.bfloat16)

        even = jnp.concatenate([dft(x0 + x1 + x2 + x3, tables[0]), dft(x0 - x1 + x2 - x3, tables[1])], axis=-1)
        odd = dft(jnp.concatenate([x0 - x2, x1 - x3], axis=-1), tables[2])
        even, odd = (part.reshape(count, local_inputs, 2, 2, channels // 4) for part in (even, odd))
        return jnp.stack([even[:, :, 0], odd[:, :, 0], even[:, :, 1], odd[:, :, 1]], axis=2)

    later = channelize(frames, spectra_dev - (lags - 1))
    head = channelize(jnp.concatenate([previous, frames[: 2 * (lags - 1)]], axis=0), lags - 1)
    spectra = jnp.concatenate([head, later], axis=0).transpose(4, 2, 1, 3, 0)
    spectra = spectra.reshape(channels, local_inputs, 2 * spectra_dev)
    packed = spectra.reshape(groups, per_group * local_inputs, 2 * spectra_dev)
    got = lax.all_to_all(packed, ("wide", "tm"), 0, 0, tiled=True)
    got = got.reshape(widen, ranks, per_group * local_inputs, 2 * spectra_dev)
    norm_factor = 1.0 / (spectra_dev * ranks)
    grams = channel_grams(got, norm_factor, per_group)
    back = lax.all_to_all(grams, "tm", 0, 0, tiled=True)
    rows = back.shape[3]
    return back.transpose(3, 1, 0, 2, 4).reshape(rows, 2, ranks * per_group, back.shape[4])


def gram_kernel(scale, x_ref, o_ref):
    widen, ranks, stacked, depth = x_ref.shape
    groups = o_ref.shape[2]
    local_inputs = stacked // groups
    inputs = widen * local_inputs
    half = depth // 2
    lane = lax.broadcasted_iota(jnp.int32, (inputs, depth), 1)
    sign = jnp.where(lane < half, -1.0, 1.0).astype(jnp.float32)
    rows = inputs // ranks
    accs = [jnp.zeros((inputs, 2 * inputs), jnp.float32) for _ in range(groups)]
    for t in range(ranks):
        block = x_ref[:, t, :, :].astype(jnp.float32)
        for c in range(groups):
            x = block[:, c * local_inputs : (c + 1) * local_inputs, :].reshape(inputs, depth)
            rot = pltpu.roll(x, half, 1) * sign
            y = jnp.concatenate([x, rot], axis=0).astype(jnp.bfloat16)
            accs[c] = accs[c] + lax.dot_general(
                x.astype(jnp.bfloat16), y, (((1,), (1,)), ((), ())),
                preferred_element_type=jnp.float32,
            )
    for c in range(groups):
        acc = accs[c] * scale
        o_ref[:, 0, c, :, :] = acc[:, :inputs].reshape(ranks, rows, inputs)
        o_ref[:, 1, c, :, :] = acc[:, inputs:].reshape(ranks, rows, inputs)


def channel_grams(got, scale, groups):
    widen, ranks, stacked, depth = got.shape
    inputs = widen * stacked // groups
    rows = inputs // ranks
    flops = 2 * groups * ranks * inputs * 2 * inputs * depth
    return pl.pallas_call(
        lambda x_ref, o_ref: gram_kernel(scale, x_ref, o_ref),
        out_shape=jax.ShapeDtypeStruct((ranks, 2, groups, rows, inputs), jnp.float32),
        in_specs=[pl.BlockSpec(memory_space=pltpu.VMEM)],
        out_specs=pl.BlockSpec(memory_space=pltpu.VMEM),
        cost_estimate=pl.CostEstimate(
            flops=flops, transcendentals=0, bytes_accessed=got.size * 2 + 2 * groups * inputs * inputs * 4
        ),
    )(got)


def solution(mesh):
    placed = (P("wide", "tm"), P())
    return jax.shard_map(
        shards, mesh=mesh, in_specs=placed, out_specs=P("tm", None, "wide", None), check_vma=False
    )
```

```python
import numpy as np
import jax
import jax.numpy as jnp
from jax import lax
from jax.experimental import pallas as pl
from jax.experimental.pallas import tpu as pltpu
from jax.sharding import PartitionSpec as P

FIR_SCALE = 2.0 ** (-12)


def shifted(array, axis, by):
    devices = lax.axis_size(axis)
    pairs = [(i, i + by) for i in range(devices) if 0 <= i + by < devices]
    return lax.ppermute(array, axis, pairs)


def radix4_factors(length, channels, split):
    quarter = length // 4
    k = (4 * np.arange(channels // 4)[None, :] + np.arange(4)[:, None]).reshape(1, channels)
    hi = np.arange(quarter // split)[:, None] * split * k % length
    lo = np.arange(split)[:, None] * k % length
    angles = [2.0 * np.pi / length * hi, 2.0 * np.pi / length * lo]
    return [f(angle).astype(np.float32) for angle in angles for f in (np.cos, np.sin)]


def radix4_tables(length, channels):
    split = 16
    ch, sh, cl, sl = (jnp.asarray(t) for t in radix4_factors(length, channels, split))
    quarter = length // 4
    cos = (ch[:, None, :] * cl[None, :, :] - sh[:, None, :] * sl[None, :, :]).reshape(quarter, channels)
    sin = (sh[:, None, :] * cl[None, :, :] + ch[:, None, :] * sl[None, :, :]).reshape(quarter, channels)
    cos = cos * length ** (-0.5)
    sin = sin * length ** (-0.5)
    per_q = channels // 4
    c0, c1, c2, c3 = (cos[:, q * per_q : (q + 1) * per_q] for q in range(4))
    s0, s1, s2, s3 = (sin[:, q * per_q : (q + 1) * per_q] for q in range(4))
    zero = jnp.zeros_like(c0)
    even = jnp.block([[c0, -s0, zero, zero], [zero, zero, c2, -s2]])
    odd = jnp.block([[c1, -s1, c3, -s3], [-s1, -c1, s3, c3]])
    return even, odd


def shards(voltages, taps):
    local_inputs = voltages.shape[0]
    length = taps.shape[1]
    lags = taps.shape[0]
    spectra_dev = voltages.shape[1] // length
    channels = length // 2
    widen = lax.axis_size("wide")
    ranks = lax.axis_size("tm")
    groups = widen * ranks
    per_group = channels // groups

    frames = voltages.reshape(local_inputs, spectra_dev, length).transpose(1, 0, 2)
    frames = frames.astype(jnp.bfloat16)
    taps_float = taps.astype(jnp.float32)
    tables = radix4_tables(length, channels)
    quarter = length // 4

    def polyphase(extended, count):
        extended = extended.astype(jnp.float32)
        filtered = taps_float[0] * extended[lags - 1 : lags - 1 + count]
        for lag in range(1, lags):
            filtered = filtered + taps_float[lag] * extended[lags - 1 - lag : lags - 1 - lag + count]
        return filtered * FIR_SCALE

    def channelize(filtered, count):
        x0, x1, x2, x3 = (filtered[..., m * quarter : (m + 1) * quarter] for m in range(4))
        inputs = [
            jnp.concatenate([x0 + x1 + x2 + x3, x0 - x1 + x2 - x3], axis=-1),
            jnp.concatenate([x0 - x2, x1 - x3], axis=-1),
        ]
        even, odd = (
            jnp.einsum(
                "sin,nm->sim",
                lhs,
                table,
                precision=lax.Precision.HIGH,
                preferred_element_type=jnp.float32,
            )
            .astype(jnp.bfloat16)
            .reshape(count, local_inputs, 2, 2, channels // 4)
            for lhs, table in zip(inputs, tables)
        )
        return jnp.stack([even[:, :, 0], odd[:, :, 0], even[:, :, 1], odd[:, :, 1]], axis=2)

    count = spectra_dev - (lags - 1)
    filtered = polyphase(frames, count)
    tail, filtered = lax.optimization_barrier((frames[spectra_dev - (lags - 1) :], filtered))
    previous = shifted(tail, "tm", 1)
    later = channelize(filtered, count)
    head_frames = jnp.concatenate([previous, frames[: 2 * (lags - 1)]], axis=0)
    head = channelize(polyphase(head_frames, lags - 1), lags - 1)
    spectra = jnp.concatenate([head, later], axis=0).transpose(4, 2, 1, 3, 0)
    spectra = spectra.reshape(channels, local_inputs, 2 * spectra_dev)
    packed = spectra.reshape(groups, per_group * local_inputs, 2 * spectra_dev)
    got = lax.all_to_all(packed, ("wide", "tm"), 0, 0, tiled=True)
    got = got.reshape(widen, ranks, per_group * local_inputs, 2 * spectra_dev)
    norm_factor = 1.0 / (spectra_dev * ranks)
    grams = channel_grams(got, norm_factor, per_group)
    back = lax.all_to_all(grams, "tm", 0, 0, tiled=True)
    rows = back.shape[3]
    return back.transpose(3, 1, 0, 2, 4).reshape(rows, 2, ranks * per_group, back.shape[4])


def gram_kernel(scale, x_ref, o_ref):
    widen, ranks, stacked, depth = x_ref.shape
    groups = o_ref.shape[2]
    local_inputs = stacked // groups
    inputs = widen * local_inputs
    half = depth // 2
    lane = lax.broadcasted_iota(jnp.int32, (inputs, depth), 1)
    sign = jnp.where(lane < half, -1.0, 1.0).astype(jnp.float32)
    rows = inputs // ranks
    accs = [jnp.zeros((inputs, 2 * inputs), jnp.float32) for _ in range(groups)]
    for t in range(ranks):
        block = x_ref[:, t, :, :].astype(jnp.float32)
        for c in range(groups):
            x = block[:, c * local_inputs : (c + 1) * local_inputs, :].reshape(inputs, depth)
            rot = pltpu.roll(x, half, 1) * sign
            y = jnp.concatenate([x, rot], axis=0).astype(jnp.bfloat16)
            accs[c] = accs[c] + lax.dot_general(
                x.astype(jnp.bfloat16), y, (((1,), (1,)), ((), ())),
                preferred_element_type=jnp.float32,
            )
    for c in range(groups):
        acc = accs[c] * scale
        o_ref[:, 0, c, :, :] = acc[:, :inputs].reshape(ranks, rows, inputs)
        o_ref[:, 1, c, :, :] = acc[:, inputs:].reshape(ranks, rows, inputs)


def channel_grams(got, scale, groups):
    widen, ranks, stacked, depth = got.shape
    inputs = widen * stacked // groups
    rows = inputs // ranks
    flops = 2 * groups * ranks * inputs * 2 * inputs * depth
    return pl.pallas_call(
        lambda x_ref, o_ref: gram_kernel(scale, x_ref, o_ref),
        out_shape=jax.ShapeDtypeStruct((ranks, 2, groups, rows, inputs), jnp.float32),
        in_specs=[pl.BlockSpec(memory_space=pltpu.VMEM)],
        out_specs=pl.BlockSpec(memory_space=pltpu.VMEM),
        cost_estimate=pl.CostEstimate(
            flops=flops, transcendentals=0, bytes_accessed=got.size * 2 + 2 * groups * inputs * inputs * 4
        ),
    )(got)


def solution(mesh):
    placed = (P("wide", "tm"), P())
    return jax.shard_map(
        shards, mesh=mesh, in_specs=placed, out_specs=P("tm", None, "wide", None), check_vma=False
    )
```

```python
import numpy as np
import jax
import jax.numpy as jnp
from jax import lax
from jax.experimental import pallas as pl
from jax.experimental.pallas import tpu as pltpu
from jax.sharding import PartitionSpec as P

FIR_SCALE = 2.0 ** (-12)


def shifted(array, axis, by):
    devices = lax.axis_size(axis)
    pairs = [(i, i + by) for i in range(devices) if 0 <= i + by < devices]
    return lax.ppermute(array, axis, pairs)


def radix4_factors(length, channels, split):
    quarter = length // 4
    column = lax.broadcasted_iota(jnp.int32, (1, channels), 1)
    k = 4 * (column % (channels // 4)) + column // (channels // 4)
    hi = (lax.broadcasted_iota(jnp.int32, (quarter // split, 1), 0) * split * k) % length
    lo = (lax.broadcasted_iota(jnp.int32, (split, 1), 0) * k) % length
    angles = [(2.0 * np.pi / length) * step.astype(jnp.float32) for step in (hi, lo)]
    return [f(angle) for angle in angles for f in (jnp.cos, jnp.sin)]


def radix4_tables(length, channels):
    split = 16
    ch, sh, cl, sl = radix4_factors(length, channels, split)
    quarter = length // 4
    cos = (ch[:, None, :] * cl[None, :, :] - sh[:, None, :] * sl[None, :, :]).reshape(quarter, channels)
    sin = (sh[:, None, :] * cl[None, :, :] + ch[:, None, :] * sl[None, :, :]).reshape(quarter, channels)
    cos = cos * length ** (-0.5)
    sin = sin * length ** (-0.5)
    per_q = channels // 4
    c0, c1, c2, c3 = (cos[:, q * per_q : (q + 1) * per_q] for q in range(4))
    s0, s1, s2, s3 = (sin[:, q * per_q : (q + 1) * per_q] for q in range(4))
    zero = jnp.zeros_like(c0)
    even = jnp.block([[c0, -s0, zero, zero], [zero, zero, c2, -s2]])
    odd = jnp.block([[c1, -s1, c3, -s3], [-s1, -c1, s3, c3]])
    return even, odd


def shards(voltages, taps):
    local_inputs = voltages.shape[0]
    length = taps.shape[1]
    lags = taps.shape[0]
    spectra_dev = voltages.shape[1] // length
    channels = length // 2
    widen = lax.axis_size("wide")
    ranks = lax.axis_size("tm")
    groups = widen * ranks
    per_group = channels // groups

    frames = voltages.reshape(local_inputs, spectra_dev, length).transpose(1, 0, 2)
    frames = frames.astype(jnp.bfloat16)
    previous = shifted(frames[spectra_dev - (lags - 1) :], "tm", 1)
    taps_float = taps.astype(jnp.float32)
    tables = radix4_tables(length, channels)
    quarter = length // 4

    def channelize(extended, count):
        extended = extended.astype(jnp.float32)
        filtered = taps_float[0] * extended[lags - 1 : lags - 1 + count]
        for lag in range(1, lags):
            filtered = filtered + taps_float[lag] * extended[lags - 1 - lag : lags - 1 - lag + count]
        filtered = filtered * FIR_SCALE
        x0, x1, x2, x3 = (filtered[..., m * quarter : (m + 1) * quarter] for m in range(4))
        inputs = [
            jnp.concatenate([x0 + x1 + x2 + x3, x0 - x1 + x2 - x3], axis=-1),
            jnp.concatenate([x0 - x2, x1 - x3], axis=-1),
        ]
        even, odd = (
            jnp.einsum(
                "sin,nm->sim",
                lhs,
                table,
                precision=lax.Precision.HIGH,
                preferred_element_type=jnp.float32,
            )
            .astype(jnp.bfloat16)
            .reshape(count, local_inputs, 2, 2, channels // 4)
            for lhs, table in zip(inputs, tables)
        )
        return jnp.stack([even[:, :, 0], odd[:, :, 0], even[:, :, 1], odd[:, :, 1]], axis=2)

    later = channelize(frames, spectra_dev - (lags - 1))
    head = channelize(jnp.concatenate([previous, frames[: 2 * (lags - 1)]], axis=0), lags - 1)
    spectra = jnp.concatenate([head, later], axis=0).transpose(4, 2, 1, 3, 0)
    spectra = spectra.reshape(channels, local_inputs, 2 * spectra_dev)
    packed = spectra.reshape(groups, per_group * local_inputs, 2 * spectra_dev)
    got = lax.all_to_all(packed, ("wide", "tm"), 0, 0, tiled=True)
    got = got.reshape(widen, ranks, per_group * local_inputs, 2 * spectra_dev)
    norm_factor = 1.0 / (spectra_dev * ranks)
    grams = channel_grams(got, norm_factor, per_group)
    back = lax.all_to_all(grams, "tm", 0, 0, tiled=True)
    rows = back.shape[3]
    return back.transpose(3, 1, 0, 2, 4).reshape(rows, 2, ranks * per_group, back.shape[4])


def gram_kernel(scale, x_ref, o_ref):
    widen, ranks, stacked, depth = x_ref.shape
    groups = o_ref.shape[2]
    local_inputs = stacked // groups
    inputs = widen * local_inputs
    half = depth // 2
    lane = lax.broadcasted_iota(jnp.int32, (inputs, depth), 1)
    sign = jnp.where(lane < half, -1.0, 1.0).astype(jnp.float32)
    rows = inputs // ranks
    accs = [jnp.zeros((inputs, 2 * inputs), jnp.float32) for _ in range(groups)]
    for t in range(ranks):
        block = x_ref[:, t, :, :].astype(jnp.float32)
        for c in range(groups):
            x = block[:, c * local_inputs : (c + 1) * local_inputs, :].reshape(inputs, depth)
            rot = pltpu.roll(x, half, 1) * sign
            y = jnp.concatenate([x, rot], axis=0).astype(jnp.bfloat16)
            accs[c] = accs[c] + lax.dot_general(
                x.astype(jnp.bfloat16), y, (((1,), (1,)), ((), ())),
                preferred_element_type=jnp.float32,
            )
    for c in range(groups):
        acc = accs[c] * scale
        o_ref[:, 0, c, :, :] = acc[:, :inputs].reshape(ranks, rows, inputs)
        o_ref[:, 1, c, :, :] = acc[:, inputs:].reshape(ranks, rows, inputs)


def channel_grams(got, scale, groups):
    widen, ranks, stacked, depth = got.shape
    inputs = widen * stacked // groups
    rows = inputs // ranks
    flops = 2 * groups * ranks * inputs * 2 * inputs * depth
    return pl.pallas_call(
        lambda x_ref, o_ref: gram_kernel(scale, x_ref, o_ref),
        out_shape=jax.ShapeDtypeStruct((ranks, 2, groups, rows, inputs), jnp.float32),
        in_specs=[pl.BlockSpec(memory_space=pltpu.VMEM)],
        out_specs=pl.BlockSpec(memory_space=pltpu.VMEM),
        cost_estimate=pl.CostEstimate(
            flops=flops, transcendentals=0, bytes_accessed=got.size * 2 + 2 * groups * inputs * inputs * 4
        ),
    )(got)


def solution(mesh):
    placed = (P("wide", "tm"), P())
    return jax.shard_map(
        shards, mesh=mesh, in_specs=placed, out_specs=P("tm", None, "wide", None), check_vma=False
    )
```
